512 devices in a mesh: island: 32 (over y, z_hi, core), fsdp: 16 (over x, z_lo).
Axes of the slice: x: 4, y: 4, z: 16 (z_hi: 4, z_lo: 4; z = z_hi * 4 + z_lo), core: 2. Of those that a mesh axis runs over, the one named last changes fastest.
Arguments:
- hidden: bfloat16 [65536, 4096], P(('island', 'fsdp')), may hold values from -6 to 6
- query_rows: bfloat16 [65536, 4096], P(('island', 'fsdp')), may hold values from -150 to 150
- key_rows: bfloat16 [65536, 512], P(('island', 'fsdp')), may hold values from -6 to 6
- targets: bfloat16 [65536, 4096], P(('island', 'fsdp')), may hold values from -6 to 6
- segment_ids: int32 [512, 128], P(('island', 'fsdp')), may hold values from 0 to 3, never falling along the last dimension, each value on 1 to 48 neighbouring positions
- first_moment: float32 [32, 4096, 512], P('island', 'fsdp'), may hold values from -0.0020716018 to 0.0020716018
- second_moment: float32 [32, 4096, 512], P('island', 'fsdp'), may hold values from 5.9604645e-08 to 9.536743e-07
- anchor: float32 [4096, 512], P('fsdp', 'island'), may hold values from -6 to 6
- outer_momentum: float32 [4096, 512], P('fsdp', 'island'), may hold values from -0.3 to 0.3
- token_counts: int32 [32], P('island'), may hold values from 4096 to 12287
Outputs:
- new_anchor: float32 [4096, 512], P('fsdp', 'island')
- new_momentum: float32 [4096, 512], P('fsdp', 'island')
The draws below stay inside these ranges and needn't reach their ends.
Inputs may be any that keep to these rules, and one draw needn't show every extreme that they name: `segment_ids`: each row is one sequence: document numbers from 0 that never fall, each document 1 to 48 tokens, one of exactly 48.
All inputs are finite; a program needn't handle non-finite values.
Results may differ from the reference program's by a relative error of at most 0.004.
Values may be sent and summed in bfloat16 or wider, within the bound.
No kernel may reach another device: no remote copies, remote signals or barrier semaphores. Data moves between devices by JAX's collectives and lax.ppermute only.
A program may use at most 64 MiB of HBM per device.

```python
import math
import jax
import jax.numpy as jnp
import numpy as np
from jax import lax

D = 4096
KVH = 4
QPK = 8
HD = 128
TOK_DEV = 128
DOCS = 4
DOC_MOST = 48
SEQS = 512
TOKENS = 65536
N_ISLAND = 32
N_FSDP = 16


def base_keys(key):
    drawn = jnp.clip(jax.random.normal(jax.random.fold_in(key, 11), (TOKENS, KVH, HD), jnp.float32), -5.0, 5.0)
    return drawn


def draw_key_rows(key, part):
    return base_keys(key).reshape(TOKENS, KVH * HD).astype(jnp.bfloat16)


def draw_query_rows(key, part):
    drawn = jnp.clip(jax.random.normal(jax.random.fold_in(key, 13), (TOKENS, KVH, QPK, HD), jnp.float32), -5.0, 5.0)
    return drawn.reshape(TOKENS, KVH * QPK * HD).astype(jnp.bfloat16)


def set_ends(values, rng, low, top_value):
    dims = values.shape
    spot = [jax.random.randint(jax.random.fold_in(rng, axis), (), 0, dims[axis]) for axis in range(len(dims))]
    values = values.at[tuple(spot)].set(low)
    longest = dims.index(max(dims))
    spot[longest] = (spot[longest] + 1) % dims[longest]
    return values.at[tuple(spot)].set(top_value)


def levels(rng, dims, split, least, largest):
    gain = 1.0
    for dim, blocks in split:
        draws = jax.random.uniform(jax.random.fold_in(jax.random.fold_in(rng, 6), dim), (blocks,), jnp.float32, least / len(split), largest / len(split))
        gain = gain * jnp.repeat(jnp.exp(draws), dims[dim] // blocks).reshape((-1,) + (1,) * (len(dims) - 1 - dim))
    return gain


def profile(number_of, total, most, lean):
    portions = [(1 << 20) // math.isqrt(rank ** lean) + 1 for rank in range(2, number_of + 1)]
    surplus, given = total - most - (number_of - 1), [1] * (number_of - 1)
    while surplus > 0:
        movable = [i for i in range(number_of - 1) if given[i] < most]
        pool, left = sum([portions[i] for i in movable]), surplus
        for i in movable:
            extra = min(most - given[i], max(1, left * portions[i] // pool), surplus)
            given[i] = given[i] + extra
            surplus = surplus - extra
    return np.array([most] + given)


def ragged_sizes(stream_key, amount, total, reach, slope):
    if amount == 2:
        one = jax.random.randint(stream_key, (), max(1, total - reach), min(reach, total - 1) + 1)
        return jnp.stack([one, total - one])
    tallies = jnp.asarray(profile(amount, total, reach, slope), jnp.int32)
    pairs = (amount - 1) // 2
    donor, taker = tallies[1:1 + 2 * pairs:2], tallies[2:2 + 2 * pairs:2]
    room = jnp.minimum(donor - 1, reach - taker)
    shifted = jax.random.randint(jax.random.fold_in(stream_key, 1), (pairs,), 0, 1 << 20) % (room + 1)
    tallies = tallies.at[1:1 + 2 * pairs:2].set(donor - shifted).at[2:2 + 2 * pairs:2].set(taker + shifted)
    return tallies[jax.random.permutation(jax.random.fold_in(stream_key, 2), amount)]


def centred(key, shape, spread, reach, cuts=(), held_as=jnp.bfloat16):
    array = jax.random.normal(key, shape, jnp.float32) * spread
    if len(cuts) > 0:
        array = levels(key, shape, cuts, -0.22, 0.18) * array
    return jnp.clip(array, min=-reach, max=reach).astype(held_as)


def setup_inputs(seed: int = 0) -> dict:
    arg_keys = jax.random.split(jax.random.key(seed), 11)
    return {
        "hidden": centred(arg_keys[0], (TOKENS, D), 1.0, 6.0, ((0, 512),)),
        "query_rows": draw_query_rows(jax.random.fold_in(arg_keys[10], 71), 0),
        "key_rows": draw_key_rows(jax.random.fold_in(arg_keys[10], 71), 0),
        "targets": centred(arg_keys[3], (TOKENS, KVH * QPK * HD), 1.0, 6.0, ((0, 512),)),
        "segment_ids": jax.vmap(lambda own: jnp.searchsorted(jnp.cumsum(ragged_sizes(own, DOCS, TOK_DEV, DOC_MOST, 0)), jnp.arange(TOK_DEV), side="right"))(jax.random.split(arg_keys[4], SEQS)).reshape((SEQS, TOK_DEV)).astype(jnp.int32),
        "first_moment": centred(arg_keys[5], (N_ISLAND, D, KVH * HD), (1.0 / (D * TOK_DEV * N_FSDP) ** 0.5), 0.0020716018, ((0, 32), (1, 16)), jnp.float32),
        "second_moment": jnp.clip(jnp.exp(math.log(9.5367431640625e-07) - 2.7725887 * jax.random.uniform(arg_keys[6], (N_ISLAND, D, KVH * HD), jnp.float32) ** levels(arg_keys[6], (N_ISLAND, D, KVH * HD), ((0, 32), (1, 16)), -0.2, 0.2)), 5.960464477539063e-08, 9.5367431640625e-07),
        "anchor": centred(arg_keys[7], (D, KVH * HD), 1.0, 6.0, ((0, 16), (1, 32)), jnp.float32),
        "outer_momentum": centred(arg_keys[8], (D, KVH * HD), 0.05, 0.3, ((0, 16), (1, 32)), jnp.float32),
        "token_counts": set_ends(jax.random.randint(arg_keys[9], (N_ISLAND,), 4096, 12288), jax.random.fold_in(arg_keys[9], 1), 4096, 12287).astype(jnp.int32),
    }


beta_one = 0.9
beta_two = 0.95
inner_rate = 0.05
decay = 0.1
epsilon = 1e-08
outer_rate = 0.7
outer_beta = 0.9

def attention_weights(query_rows, key_rows, segments):
    count = segments.shape[0]
    length = segments.shape[1]
    queries = query_rows.astype(jnp.float32).reshape(count, length, KVH, QPK, HD)
    keyed = key_rows.astype(jnp.float32).reshape(count, length, KVH, HD)
    scores = jnp.einsum('btgjd,bsgd->bgjts', queries, keyed) * (1.0 / math.sqrt(HD))
    place = jnp.arange(length)
    causal = place[None, :] <= place[:, None]
    same = segments[:, :, None] == segments[:, None, :]
    allowed = (causal[None] & same)[:, None, None]
    scores = jnp.where(allowed, scores, -jnp.inf)
    highest = lax.optimization_barrier(jnp.max(scores, axis=-1, keepdims=True))
    expo = jnp.exp(scores - highest)
    return (expo / lax.optimization_barrier(jnp.sum(expo, axis=-1, keepdims=True))).astype(jnp.bfloat16)

def reference(hidden, query_rows, key_rows, targets, segment_ids, first_moment, second_moment, anchor, outer_momentum, token_counts):
    group_rows = N_FSDP * TOK_DEV
    scale_in = 1.0 / math.sqrt(D)
    width = KVH * HD
    block = D // N_FSDP

    def island_delta(inputs):
        local_hidden, local_queries, local_keys, local_targets, segments, first, second = inputs
        attention = attention_weights(local_queries, local_keys, segments).astype(jnp.float32)
        hidden_blocks = local_hidden.astype(jnp.float32).reshape(group_rows, N_FSDP, block)
        weight = anchor
        for inner_step in range(2):
            rounded = lax.optimization_barrier(weight.astype(jnp.bfloat16)).astype(jnp.float32)
            blocks = jnp.einsum('rnc,ncw->nrw', hidden_blocks, rounded.reshape(N_FSDP, block, width))
            block_values = lax.optimization_barrier(blocks.astype(jnp.bfloat16)).astype(jnp.float32)
            values = (lax.optimization_barrier(jnp.sum(block_values, axis=0)) * scale_in).astype(jnp.bfloat16)
            mixed = jnp.einsum('bgjts,bsgd->btgjd', attention, values.astype(jnp.float32).reshape(N_FSDP, TOK_DEV, KVH, HD))
            error = ((mixed.reshape(group_rows, KVH * QPK * HD) - local_targets.astype(jnp.float32)) / group_rows).astype(jnp.bfloat16)
            back = jnp.einsum('bgjts,btgjd->bsgd', attention, error.astype(jnp.float32).reshape(N_FSDP, TOK_DEV, KVH, QPK, HD))
            value_grad = (back.reshape(group_rows, width) * scale_in).astype(jnp.bfloat16)
            grad = jnp.dot(local_hidden.T, value_grad, preferred_element_type=jnp.float32)
            first = beta_one * first + (1.0 - beta_one) * grad
            second = beta_two * second + (1.0 - beta_two) * grad * grad
            weight = weight - inner_rate * (first / (jnp.sqrt(second) + epsilon) + decay * weight)
        return anchor - weight
    deltas = lax.map(island_delta, (hidden.reshape(N_ISLAND, group_rows, D), query_rows.reshape(N_ISLAND, group_rows, KVH * QPK * HD), key_rows.reshape(N_ISLAND, group_rows, width), targets.reshape(N_ISLAND, group_rows, KVH * QPK * HD), segment_ids.reshape(N_ISLAND, N_FSDP, TOK_DEV), first_moment, second_moment))
    counts = token_counts.astype(jnp.float32)
    average = lax.optimization_barrier(jnp.sum(counts[:, None, None] * deltas, axis=0)) / jnp.sum(counts)
    new_momentum = outer_beta * outer_momentum + average
    new_anchor = anchor - outer_rate * (average + outer_beta * new_momentum)
    return (new_anchor, new_momentum)
```

```python
import math

import jax
import jax.numpy as jnp
from jax import lax
from jax.sharding import PartitionSpec as P

KVH = 4
QPK = 8
HD = 128


beta_one = 0.9
beta_two = 0.95
inner_rate = 0.05
decay = 0.1
epsilon = 1e-08
outer_rate = 0.7
outer_beta = 0.9


def attention_weights(query_rows, key_rows, segments):
    length = segments.shape[0]
    queries = query_rows.reshape(length, KVH, QPK, HD)
    keyed = key_rows.reshape(length, KVH, HD)
    scores = jnp.einsum("tgjd,sgd->gjts", queries, keyed, preferred_element_type=jnp.float32) * (
        1.0 / math.sqrt(HD)
    )
    place = jnp.arange(length)
    allowed = (place[None, :] <= place[:, None]) & (segments[:, None] == segments[None, :])
    scores = jnp.where(allowed[None, None], scores, -jnp.inf)
    highest = jnp.max(scores, axis=-1, keepdims=True)
    expo = jnp.exp(scores - highest)
    return (expo / jnp.sum(expo, axis=-1, keepdims=True)).astype(jnp.bfloat16)


def on_device(
    hidden,
    query_rows,
    key_rows,
    targets,
    segment_ids,
    first_moment,
    second_moment,
    anchor,
    outer_momentum,
    token_counts,
):
    rows = hidden.shape[0]
    width = key_rows.shape[1]
    members = lax.axis_size("fsdp")
    group_rows = rows * members
    scale_in = 1.0 / math.sqrt(hidden.shape[1])
    attention = attention_weights(query_rows, key_rows, segment_ids[0])
    master = lax.all_gather(anchor, "island", axis=1, tiled=True)
    start_point = master
    block = master.shape[0]
    first = first_moment[0]
    second = second_moment[0]
    feature_rows = lax.all_to_all(hidden, "fsdp", split_axis=1, concat_axis=0, tiled=True)
    for inner_step in range(2):
        partial = jnp.dot(
            feature_rows, master.astype(jnp.bfloat16), preferred_element_type=jnp.float32
        ).astype(jnp.bfloat16)
        pieces = lax.all_to_all(
            partial.reshape(members, rows, width), "fsdp", split_axis=0, concat_axis=0, tiled=True
        )
        projected = jnp.sum(pieces.astype(jnp.float32), axis=0)
        values = (projected * scale_in).astype(jnp.bfloat16)
        mixed = jnp.einsum(
            "gjts,sgd->tgjd",
            attention,
            values.reshape(rows, KVH, HD),
            preferred_element_type=jnp.float32,
        )
        error = (
            (mixed.reshape(rows, KVH * QPK * HD) - targets.astype(jnp.float32)) / group_rows
        ).astype(jnp.bfloat16)
        back = jnp.einsum(
            "gjts,tgjd->sgd",
            attention,
            error.reshape(rows, KVH, QPK, HD),
            preferred_element_type=jnp.float32,
        )
        value_grad = (back.reshape(rows, width) * scale_in).astype(jnp.bfloat16)
        grad = lax.dot_general(
            feature_rows,
            lax.all_gather(value_grad, "fsdp", axis=0, tiled=True),
            (((0,), (0,)), ((), ())),
            preferred_element_type=jnp.float32,
        )
        first = beta_one * first + (1.0 - beta_one) * grad
        second = beta_two * second + (1.0 - beta_two) * grad * grad
        master = master - inner_rate * (first / (jnp.sqrt(second) + epsilon) + decay * master)
    delta = start_point - master
    groups = lax.axis_size("island")
    cols = anchor.shape[1]
    own_count = token_counts[0].astype(jnp.float32)
    weighted = jnp.concatenate(
        [own_count * delta, jnp.full((1, delta.shape[1]), own_count, jnp.float32)], axis=0
    )
    received = lax.all_to_all(
        weighted.reshape(block + 1, groups, cols), "island", split_axis=1, concat_axis=0, tiled=True
    )
    summed = jnp.sum(received.reshape(groups, block + 1, cols), axis=0)
    average = summed[:block] / summed[block:]
    new_momentum = outer_beta * outer_momentum + average
    new_anchor = anchor - outer_rate * (average + outer_beta * new_momentum)
    return (new_anchor, new_momentum)


def solution(mesh):
    in_specs = (
        P(("island", "fsdp"), None),
        P(("island", "fsdp"), None),
        P(("island", "fsdp"), None),
        P(("island", "fsdp"), None),
        P(("island", "fsdp"), None),
        P("island", "fsdp", None),
        P("island", "fsdp", None),
        P("fsdp", "island"),
        P("fsdp", "island"),
        P("island"),
    )
    out_specs = (P("fsdp", "island"), P("fsdp", "island"))
    return jax.shard_map(
        on_device, mesh=mesh, in_specs=in_specs, out_specs=out_specs, check_vma=False
    )
```

```python
import math

import jax
import jax.numpy as jnp
from jax import lax
from jax.sharding import PartitionSpec as P

KVH = 4
QPK = 8
HD = 128


beta_one = 0.9
beta_two = 0.95
inner_rate = 0.05
decay = 0.1
epsilon = 1e-08
outer_rate = 0.7
outer_beta = 0.9


def attention_weights(query_rows, key_rows, segments):
    length = segments.shape[0]
    queries = query_rows.reshape(length, KVH, QPK, HD)
    keyed = key_rows.reshape(length, KVH, HD)
    scores = jnp.einsum("tgjd,sgd->gjts", queries, keyed, preferred_element_type=jnp.float32) * (
        1.0 / math.sqrt(HD)
    )
    place = jnp.arange(length)
    allowed = (place[None, :] <= place[:, None]) & (segments[:, None] == segments[None, :])
    scores = jnp.where(allowed[None, None], scores, -jnp.inf)
    highest = jnp.max(scores, axis=-1, keepdims=True)
    expo = jnp.exp(scores - highest)
    return (expo / jnp.sum(expo, axis=-1, keepdims=True)).astype(jnp.bfloat16)


def _shift(cols, rows, dx, dz):
    return [
        (a * cols + b, ((a + dx) % rows) * cols + (b + dz) % cols)
        for a in range(rows)
        for b in range(cols)
    ]


def ring_offsets(size):
    return [0, -1, 1, -2][:size] if size == 4 else list(range(0, -size, -1))


def ring_gather(piece, rows, cols):
    def along(part, size, dx, dz):
        if size == 1:
            return [part]
        if size == 4:
            up = lax.ppermute(part, "fsdp", _shift(cols, rows, dx, dz))
            down = lax.ppermute(part, "fsdp", _shift(cols, rows, -dx, -dz))
            far = lax.ppermute(up, "fsdp", _shift(cols, rows, dx, dz))
            return [part, up, down, far]
        got = [part]
        for _ in range(size - 1):
            got.append(lax.ppermute(got[-1], "fsdp", _shift(cols, rows, dx, dz)))
        return got

    row = jnp.concatenate(along(piece, cols, 0, 1), axis=0)
    return jnp.concatenate(along(row, rows, 1, 0), axis=0)


def on_device(
    hidden,
    query_rows,
    key_rows,
    targets,
    segment_ids,
    first_moment,
    second_moment,
    anchor,
    outer_momentum,
    token_counts,
):
    rows = hidden.shape[0]
    width = key_rows.shape[1]
    members = lax.axis_size("fsdp")
    group_rows = rows * members
    scale_in = 1.0 / math.sqrt(hidden.shape[1])
    attention = attention_weights(query_rows, key_rows, segment_ids[0])
    groups = lax.axis_size("island")
    copies = jnp.broadcast_to(anchor[None], (groups,) + anchor.shape)
    master = (
        lax.all_to_all(copies, "island", split_axis=0, concat_axis=0, tiled=True)
        .transpose(1, 0, 2)
        .reshape(anchor.shape[0], groups * anchor.shape[1])
    )
    start_point = master
    block = master.shape[0]
    first = first_moment[0]
    second = second_moment[0]
    feature_rows = lax.all_to_all(hidden, "fsdp", split_axis=1, concat_axis=0, tiled=True)
    grid_cols = 4 if members % 4 == 0 else 1
    grid_rows = members // grid_cols
    me = lax.axis_index("fsdp")
    me_x, me_z = me // grid_cols, me % grid_cols
    take_x = (me_x + jnp.array(ring_offsets(grid_rows))) % grid_rows
    take_z = (me_z + jnp.array(ring_offsets(grid_cols))) % grid_cols
    order = (take_x[:, None] * grid_cols + take_z[None, :]).reshape(-1)
    ring_rows = jnp.take(
        feature_rows.reshape(members, rows, block), order, axis=0
    ).reshape(group_rows, block)
    for inner_step in range(2):
        partial = jnp.dot(
            feature_rows, master.astype(jnp.bfloat16), preferred_element_type=jnp.float32
        ).astype(jnp.bfloat16)
        pieces = lax.all_to_all(
            partial.reshape(members, rows, width), "fsdp", split_axis=0, concat_axis=0, tiled=True
        )
        projected = jnp.sum(pieces.astype(jnp.float32), axis=0)
        values = (projected * scale_in).astype(jnp.bfloat16)
        mixed = jnp.einsum(
            "gjts,sgd->tgjd",
            attention,
            values.reshape(rows, KVH, HD),
            preferred_element_type=jnp.float32,
        )
        error = (
            (mixed.reshape(rows, KVH * QPK * HD) - targets.astype(jnp.float32)) / group_rows
        ).astype(jnp.bfloat16)
        back = jnp.einsum(
            "gjts,tgjd->sgd",
            attention,
            error.reshape(rows, KVH, QPK, HD),
            preferred_element_type=jnp.float32,
        )
        value_grad = (back.reshape(rows, width) * scale_in).astype(jnp.bfloat16)
        grad = lax.dot_general(
            ring_rows,
            ring_gather(value_grad, grid_rows, grid_cols),
            (((0,), (0,)), ((), ())),
            preferred_element_type=jnp.float32,
        )
        first = beta_one * first + (1.0 - beta_one) * grad
        second = beta_two * second + (1.0 - beta_two) * grad * grad
        master = master - inner_rate * (first / (jnp.sqrt(second) + epsilon) + decay * master)
    delta = start_point - master
    cols = anchor.shape[1]
    own_count = token_counts[0].astype(jnp.float32)
    weighted = jnp.concatenate(
        [own_count * delta, jnp.full((1, delta.shape[1]), own_count, jnp.float32)], axis=0
    )
    received = lax.all_to_all(
        weighted.reshape(block + 1, groups, cols), "island", split_axis=1, concat_axis=0, tiled=True
    )
    summed = jnp.sum(received.reshape(groups, block + 1, cols), axis=0)
    average = summed[:block] / summed[block:]
    new_momentum = outer_beta * outer_momentum + average
    new_anchor = anchor - outer_rate * (average + outer_beta * new_momentum)
    return (new_anchor, new_momentum)


def solution(mesh):
    in_specs = (
        P(("island", "fsdp"), None),
        P(("island", "fsdp"), None),
        P(("island", "fsdp"), None),
        P(("island", "fsdp"), None),
        P(("island", "fsdp"), None),
        P("island", "fsdp", None),
        P("island", "fsdp", None),
        P("fsdp", "island"),
        P("fsdp", "island"),
        P("island"),
    )
    out_specs = (P("fsdp", "island"), P("fsdp", "island"))
    return jax.shard_map(
        on_device, mesh=mesh, in_specs=in_specs, out_specs=out_specs, check_vma=False
    )
```

```python
import math

import jax
import jax.numpy as jnp
from jax import lax
from jax.sharding import PartitionSpec as P

KVH = 4
QPK = 8
HD = 128
CHUNKS = 2


beta_one = 0.9
beta_two = 0.95
inner_rate = 0.05
decay = 0.1
epsilon = 1e-08
outer_rate = 0.7
outer_beta = 0.9


def attention_weights(query_rows, key_rows, segments):
    length = segments.shape[0]
    queries = query_rows.reshape(length, KVH, QPK, HD)
    keyed = key_rows.reshape(length, KVH, HD)
    scores = jnp.einsum("tgjd,sgd->gjts", queries, keyed, preferred_element_type=jnp.float32) * (
        1.0 / math.sqrt(HD)
    )
    place = jnp.arange(length)
    allowed = (place[None, :] <= place[:, None]) & (segments[:, None] == segments[None, :])
    scores = jnp.where(allowed[None, None], scores, -jnp.inf)
    highest = jnp.max(scores, axis=-1, keepdims=True)
    expo = jnp.exp(scores - highest)
    return (expo / jnp.sum(expo, axis=-1, keepdims=True)).astype(jnp.bfloat16)


def _shift(cols, rows, dx, dz):
    return [
        (a * cols + b, ((a + dx) % rows) * cols + (b + dz) % cols)
        for a in range(rows)
        for b in range(cols)
    ]


def ring_offsets(size):
    return [0, -1, 1, -2][:size] if size == 4 else list(range(0, -size, -1))


def ring_gather(piece, rows, cols):
    def along(part, size, dx, dz):
        if size == 1:
            return [part]
        if size == 4:
            up = lax.ppermute(part, "fsdp", _shift(cols, rows, dx, dz))
            down = lax.ppermute(part, "fsdp", _shift(cols, rows, -dx, -dz))
            far = lax.ppermute(up, "fsdp", _shift(cols, rows, dx, dz))
            return [part, up, down, far]
        got = [part]
        for _ in range(size - 1):
            got.append(lax.ppermute(got[-1], "fsdp", _shift(cols, rows, dx, dz)))
        return got

    row = jnp.concatenate(along(piece, cols, 0, 1), axis=0)
    return jnp.concatenate(along(row, rows, 1, 0), axis=0)


def on_device(
    hidden,
    query_rows,
    key_rows,
    targets,
    segment_ids,
    first_moment,
    second_moment,
    anchor,
    outer_momentum,
    token_counts,
):
    rows = hidden.shape[0]
    width = key_rows.shape[1]
    members = lax.axis_size("fsdp")
    group_rows = rows * members
    scale_in = 1.0 / math.sqrt(hidden.shape[1])
    attention = attention_weights(query_rows, key_rows, segment_ids[0])
    groups = lax.axis_size("island")
    copies = jnp.broadcast_to(anchor[None], (groups,) + anchor.shape)
    master = (
        lax.all_to_all(copies, "island", split_axis=0, concat_axis=0, tiled=True)
        .transpose(1, 0, 2)
        .reshape(anchor.shape[0], groups * anchor.shape[1])
    )
    start_point = master
    block = master.shape[0]
    first = first_moment[0]
    second = second_moment[0]
    feature_rows = lax.all_to_all(hidden, "fsdp", split_axis=1, concat_axis=0, tiled=True)
    grid_cols = 4 if members % 4 == 0 else 1
    grid_rows = members // grid_cols
    me = lax.axis_index("fsdp")
    me_x, me_z = me // grid_cols, me % grid_cols
    take_x = (me_x + jnp.array(ring_offsets(grid_rows))) % grid_rows
    take_z = (me_z + jnp.array(ring_offsets(grid_cols))) % grid_cols
    order = (take_x[:, None] * grid_cols + take_z[None, :]).reshape(-1)
    ring_rows = jnp.take(
        feature_rows.reshape(members, rows, block), order, axis=0
    ).reshape(group_rows, block)
    heads = KVH // CHUNKS
    span = heads * HD
    wide = heads * QPK * HD
    weights = [master[:, c * span : (c + 1) * span] for c in range(CHUNKS)]
    firsts = [first[:, c * span : (c + 1) * span] for c in range(CHUNKS)]
    seconds = [second[:, c * span : (c + 1) * span] for c in range(CHUNKS)]
    for inner_step in range(2):
        for c in range(CHUNKS):
            partial = jnp.dot(
                feature_rows, weights[c].astype(jnp.bfloat16), preferred_element_type=jnp.float32
            ).astype(jnp.bfloat16)
            pieces = lax.all_to_all(
                partial.reshape(members, rows, span), "fsdp", split_axis=0, concat_axis=0, tiled=True
            )
            projected = jnp.sum(pieces.astype(jnp.float32), axis=0)
            values = (projected * scale_in).astype(jnp.bfloat16)
            own_attention = attention[c * heads : (c + 1) * heads]
            mixed = jnp.einsum(
                "gjts,sgd->tgjd",
                own_attention,
                values.reshape(rows, heads, HD),
                preferred_element_type=jnp.float32,
            )
            error = (
                (
                    mixed.reshape(rows, wide)
                    - targets[:, c * wide : (c + 1) * wide].astype(jnp.float32)
                )
                / group_rows
            ).astype(jnp.bfloat16)
            back = jnp.einsum(
                "gjts,tgjd->sgd",
                own_attention,
                error.reshape(rows, heads, QPK, HD),
                preferred_element_type=jnp.float32,
            )
            value_grad = (back.reshape(rows, span) * scale_in).astype(jnp.bfloat16)
            grad = lax.dot_general(
                ring_rows,
                ring_gather(value_grad, grid_rows, grid_cols),
                (((0,), (0,)), ((), ())),
                preferred_element_type=jnp.float32,
            )
            firsts[c] = beta_one * firsts[c] + (1.0 - beta_one) * grad
            seconds[c] = beta_two * seconds[c] + (1.0 - beta_two) * grad * grad
            weights[c] = weights[c] - inner_rate * (
                firsts[c] / (jnp.sqrt(seconds[c]) + epsilon) + decay * weights[c]
            )
    master = jnp.concatenate(weights, axis=1)
    delta = start_point - master
    cols = anchor.shape[1]
    own_count = token_counts[0].astype(jnp.float32)
    weighted = jnp.concatenate(
        [own_count * delta, jnp.full((1, delta.shape[1]), own_count, jnp.float32)], axis=0
    )
    received = lax.all_to_all(
        weighted.reshape(block + 1, groups, cols), "island", split_axis=1, concat_axis=0, tiled=True
    )
    summed = jnp.sum(received.reshape(groups, block + 1, cols), axis=0)
    average = summed[:block] / summed[block:]
    new_momentum = outer_beta * outer_momentum + average
    new_anchor = anchor - outer_rate * (average + outer_beta * new_momentum)
    return (new_anchor, new_momentum)


def solution(mesh):
    in_specs = (
        P(("island", "fsdp"), None),
        P(("island", "fsdp"), None),
        P(("island", "fsdp"), None),
        P(("island", "fsdp"), None),
        P(("island", "fsdp"), None),
        P("island", "fsdp", None),
        P("island", "fsdp", None),
        P("fsdp", "island"),
        P("fsdp", "island"),
        P("island"),
    )
    out_specs = (P("fsdp", "island"), P("fsdp", "island"))
    return jax.shard_map(
        on_device, mesh=mesh, in_specs=in_specs, out_specs=out_specs, check_vma=False
    )
```

```python
import math

import jax
import jax.numpy as jnp
from jax import lax
from jax.sharding import PartitionSpec as P

KVH = 4
QPK = 8
HD = 128


beta_one = 0.9
beta_two = 0.95
inner_rate = 0.05
decay = 0.1
epsilon = 1e-08
outer_rate = 0.7
outer_beta = 0.9


def attention_weights(query_rows, key_rows, segments):
    length = segments.shape[0]
    queries = query_rows.reshape(length, KVH, QPK, HD)
    keyed = key_rows.reshape(length, KVH, HD)
    scores = jnp.einsum("tgjd,sgd->gjts", queries, keyed, preferred_element_type=jnp.float32) * (
        1.0 / math.sqrt(HD)
    )
    place = jnp.arange(length)
    allowed = (place[None, :] <= place[:, None]) & (segments[:, None] == segments[None, :])
    scores = jnp.where(allowed[None, None], scores, -jnp.inf)
    highest = jnp.max(scores, axis=-1, keepdims=True)
    expo = jnp.exp(scores - highest)
    return (expo / jnp.sum(expo, axis=-1, keepdims=True)).astype(jnp.bfloat16)


def _shift(cols, rows, dx, dz):
    return [
        (a * cols + b, ((a + dx) % rows) * cols + (b + dz) % cols)
        for a in range(rows)
        for b in range(cols)
    ]


def ring_offsets(size):
    return [0, -1, 1, -2][:size] if size == 4 else list(range(0, -size, -1))


def ring_gather(piece, rows, cols):
    def along(part, size, dx, dz):
        if size == 1:
            return [part]
        if size == 4:
            up = lax.ppermute(part, "fsdp", _shift(cols, rows, dx, dz))
            down = lax.ppermute(part, "fsdp", _shift(cols, rows, -dx, -dz))
            far = lax.ppermute(up, "fsdp", _shift(cols, rows, dx, dz))
            return [part, up, down, far]
        got = [part]
        for _ in range(size - 1):
            got.append(lax.ppermute(got[-1], "fsdp", _shift(cols, rows, dx, dz)))
        return got

    row = jnp.concatenate(along(piece, cols, 0, 1), axis=0)
    return jnp.concatenate(along(row, rows, 1, 0), axis=0)


def on_device(
    hidden,
    query_rows,
    key_rows,
    targets,
    segment_ids,
    first_moment,
    second_moment,
    anchor,
    outer_momentum,
    token_counts,
):
    rows = hidden.shape[0]
    width = key_rows.shape[1]
    members = lax.axis_size("fsdp")
    group_rows = rows * members
    scale_in = 1.0 / math.sqrt(hidden.shape[1])
    attention = attention_weights(query_rows, key_rows, segment_ids[0])
    groups = lax.axis_size("island")
    master = lax.all_gather(anchor, "island", axis=1, tiled=True)
    start_point = master
    block = master.shape[0]
    first = first_moment[0]
    second = second_moment[0]
    feature_rows = lax.all_to_all(hidden, "fsdp", split_axis=1, concat_axis=0, tiled=True)
    grid_cols = 4 if members % 4 == 0 else 1
    grid_rows = members // grid_cols
    me = lax.axis_index("fsdp")
    me_x, me_z = me // grid_cols, me % grid_cols
    take_x = (me_x + jnp.array(ring_offsets(grid_rows))) % grid_rows
    take_z = (me_z + jnp.array(ring_offsets(grid_cols))) % grid_cols
    order = (take_x[:, None] * grid_cols + take_z[None, :]).reshape(-1)
    ring_rows = jnp.take(
        feature_rows.reshape(members, rows, block), order, axis=0
    ).reshape(group_rows, block)
    for inner_step in range(2):
        partial = jnp.dot(
            feature_rows, master.astype(jnp.bfloat16), preferred_element_type=jnp.float32
        ).astype(jnp.bfloat16)
        pieces = lax.all_to_all(
            partial.reshape(members, rows, width), "fsdp", split_axis=0, concat_axis=0, tiled=True
        )
        projected = jnp.sum(pieces.astype(jnp.float32), axis=0)
        values = (projected * scale_in).astype(jnp.bfloat16)
        mixed = jnp.einsum(
            "gjts,sgd->tgjd",
            attention,
            values.reshape(rows, KVH, HD),
            preferred_element_type=jnp.float32,
        )
        error = (
            (mixed.reshape(rows, KVH * QPK * HD) - targets.astype(jnp.float32)) / group_rows
        ).astype(jnp.bfloat16)
        back = jnp.einsum(
            "gjts,tgjd->sgd",
            attention,
            error.reshape(rows, KVH, QPK, HD),
            preferred_element_type=jnp.float32,
        )
        value_grad = (back.reshape(rows, width) * scale_in).astype(jnp.bfloat16)
        grad = lax.dot_general(
            ring_rows,
            ring_gather(value_grad, grid_rows, grid_cols),
            (((0,), (0,)), ((), ())),
            preferred_element_type=jnp.float32,
        )
        first = beta_one * first + (1.0 - beta_one) * grad
        second = beta_two * second + (1.0 - beta_two) * grad * grad
        master = master - inner_rate * (first / (jnp.sqrt(second) + epsilon) + decay * master)
    delta = start_point - master
    cols = anchor.shape[1]
    own_count = token_counts[0].astype(jnp.float32)
    count_high = own_count.astype(jnp.bfloat16)
    count_low = (own_count - count_high.astype(jnp.float32)).astype(jnp.bfloat16)
    sent = jnp.concatenate(
        [
            delta.astype(jnp.bfloat16),
            jnp.full((1, delta.shape[1]), count_high, jnp.bfloat16),
            jnp.full((1, delta.shape[1]), count_low, jnp.bfloat16),
        ],
        axis=0,
    )
    received = lax.all_to_all(
        sent.reshape(block + 2, groups, cols), "island", split_axis=1, concat_axis=0, tiled=True
    ).reshape(groups, block + 2, cols).astype(jnp.float32)
    counts = received[:, block] + received[:, block + 1]
    total = jnp.sum(counts, axis=0)
    average = jnp.sum(counts[:, None, :] * received[:, :block], axis=0) / total
    new_momentum = outer_beta * outer_momentum + average
    new_anchor = anchor - outer_rate * (average + outer_beta * new_momentum)
    return (new_anchor, new_momentum)


def solution(mesh):
    in_specs = (
        P(("island", "fsdp"), None),
        P(("island", "fsdp"), None),
        P(("island", "fsdp"), None),
        P(("island", "fsdp"), None),
        P(("island", "fsdp"), None),
        P("island", "fsdp", None),
        P("island", "fsdp", None),
        P("fsdp", "island"),
        P("fsdp", "island"),
        P("island"),
    )
    out_specs = (P("fsdp", "island"), P("fsdp", "island"))
    return jax.shard_map(
        on_device, mesh=mesh, in_specs=in_specs, out_specs=out_specs, check_vma=False
    )
```

```python
import math

import jax
import jax.numpy as jnp
from jax import lax
from jax.sharding import PartitionSpec as P

KVH = 4
QPK = 8
HD = 128


beta_one = 0.9
beta_two = 0.95
inner_rate = 0.05
decay = 0.1
epsilon = 1e-08
outer_rate = 0.7
outer_beta = 0.9


def attention_weights(query_rows, key_rows, segments):
    length = segments.shape[0]
    queries = query_rows.reshape(length, KVH, QPK, HD)
    keyed = key_rows.reshape(length, KVH, HD)
    scores = jnp.einsum("tgjd,sgd->gjts", queries, keyed, preferred_element_type=jnp.float32) * (
        1.0 / math.sqrt(HD)
    )
    place = jnp.arange(length)
    allowed = (place[None, :] <= place[:, None]) & (segments[:, None] == segments[None, :])
    scores = jnp.where(allowed[None, None], scores, -jnp.inf)
    highest = jnp.max(scores, axis=-1, keepdims=True)
    expo = jnp.exp(scores - highest)
    return (expo / jnp.sum(expo, axis=-1, keepdims=True)).astype(jnp.bfloat16)


def _shift(cols, rows, dx, dz):
    return [
        (a * cols + b, ((a + dx) % rows) * cols + (b + dz) % cols)
        for a in range(rows)
        for b in range(cols)
    ]


def ring_offsets(size):
    return [0, -1, 1, -2][:size] if size == 4 else list(range(0, -size, -1))


def ring_gather(piece, rows, cols):
    def along(part, size, dx, dz):
        if size == 1:
            return [part]
        if size == 4:
            up = lax.ppermute(part, "fsdp", _shift(cols, rows, dx, dz))
            down = lax.ppermute(part, "fsdp", _shift(cols, rows, -dx, -dz))
            far = lax.ppermute(up, "fsdp", _shift(cols, rows, dx, dz))
            return [part, up, down, far]
        got = [part]
        for _ in range(size - 1):
            got.append(lax.ppermute(got[-1], "fsdp", _shift(cols, rows, dx, dz)))
        return got

    row = jnp.concatenate(along(piece, cols, 0, 1), axis=0)
    return jnp.concatenate(along(row, rows, 1, 0), axis=0)


def ring_exchange(hidden, rows, cols, block):
    me = lax.axis_index("fsdp")
    me_x, me_z = me // cols, me % cols
    tokens = hidden.shape[0]
    mine = hidden.reshape(tokens, rows, cols, block).transpose(1, 2, 0, 3)
    stage = []
    for dz in [0, 1, -1, 2]:
        part = lax.dynamic_index_in_dim(mine, (me_z + dz) % cols, axis=1, keepdims=False)
        if dz:
            part = lax.ppermute(part, "fsdp", _shift(cols, rows, 0, dz))
        stage.append(part)
    gathered = jnp.stack(stage, axis=1)
    out = []
    for dx in [0, 1, -1, 2]:
        part = lax.dynamic_index_in_dim(gathered, (me_x + dx) % rows, axis=0, keepdims=False)
        if dx:
            part = lax.ppermute(part, "fsdp", _shift(cols, rows, dx, 0))
        out.append(part)
    return jnp.stack(out, axis=0).reshape(rows * cols * tokens, block)


def on_device(
    hidden,
    query_rows,
    key_rows,
    targets,
    segment_ids,
    first_moment,
    second_moment,
    anchor,
    outer_momentum,
    token_counts,
):
    rows = hidden.shape[0]
    width = key_rows.shape[1]
    members = lax.axis_size("fsdp")
    group_rows = rows * members
    scale_in = 1.0 / math.sqrt(hidden.shape[1])
    attention = attention_weights(query_rows, key_rows, segment_ids[0])
    groups = lax.axis_size("island")
    copies = jnp.broadcast_to(anchor[None], (groups,) + anchor.shape)
    master = (
        lax.all_to_all(copies, "island", split_axis=0, concat_axis=0, tiled=True)
        .transpose(1, 0, 2)
        .reshape(anchor.shape[0], groups * anchor.shape[1])
    )
    start_point = master
    block = master.shape[0]
    first = first_moment[0]
    second = second_moment[0]
    grid_cols = 4 if members % 4 == 0 else 1
    grid_rows = members // grid_cols
    me = lax.axis_index("fsdp")
    me_x, me_z = me // grid_cols, me % grid_cols
    take_x = (me_x + jnp.array(ring_offsets(grid_rows))) % grid_rows
    take_z = (me_z + jnp.array(ring_offsets(grid_cols))) % grid_cols
    order = (take_x[:, None] * grid_cols + take_z[None, :]).reshape(-1)
    if grid_rows == 4 and grid_cols == 4:
        ring_rows = ring_exchange(hidden, grid_rows, grid_cols, block)
        feature_rows = jnp.take(
            ring_rows.reshape(members, rows, block), jnp.argsort(order), axis=0
        ).reshape(group_rows, block)
    else:
        feature_rows = lax.all_to_all(hidden, "fsdp", split_axis=1, concat_axis=0, tiled=True)
        ring_rows = jnp.take(
            feature_rows.reshape(members, rows, block), order, axis=0
        ).reshape(group_rows, block)
    for inner_step in range(2):
        partial = jnp.dot(
            feature_rows, master.astype(jnp.bfloat16), preferred_element_type=jnp.float32
        ).astype(jnp.bfloat16)
        pieces = lax.all_to_all(
            partial.reshape(members, rows, width), "fsdp", split_axis=0, concat_axis=0, tiled=True
        )
        projected = jnp.sum(pieces.astype(jnp.float32), axis=0)
        values = (projected * scale_in).astype(jnp.bfloat16)
        mixed = jnp.einsum(
            "gjts,sgd->tgjd",
            attention,
            values.reshape(rows, KVH, HD),
            preferred_element_type=jnp.float32,
        )
        error = (
            (mixed.reshape(rows, KVH * QPK * HD) - targets.astype(jnp.float32)) / group_rows
        ).astype(jnp.bfloat16)
        back = jnp.einsum(
            "gjts,tgjd->sgd",
            attention,
            error.reshape(rows, KVH, QPK, HD),
            preferred_element_type=jnp.float32,
        )
        value_grad = (back.reshape(rows, width) * scale_in).astype(jnp.bfloat16)
        grad = lax.dot_general(
            ring_rows,
            ring_gather(value_grad, grid_rows, grid_cols),
            (((0,), (0,)), ((), ())),
            preferred_element_type=jnp.float32,
        )
        first = beta_one * first + (1.0 - beta_one) * grad
        second = beta_two * second + (1.0 - beta_two) * grad * grad
        master = master - inner_rate * (first / (jnp.sqrt(second) + epsilon) + decay * master)
    delta = start_point - master
    cols = anchor.shape[1]
    own_count = token_counts[0].astype(jnp.float32)
    count_high = own_count.astype(jnp.bfloat16)
    count_low = (own_count - count_high.astype(jnp.float32)).astype(jnp.bfloat16)
    sent = jnp.concatenate(
        [
            delta.astype(jnp.bfloat16),
            jnp.full((1, delta.shape[1]), count_high, jnp.bfloat16),
            jnp.full((1, delta.shape[1]), count_low, jnp.bfloat16),
        ],
        axis=0,
    )
    received = lax.all_to_all(
        sent.reshape(block + 2, groups, cols), "island", split_axis=1, concat_axis=0, tiled=True
    ).reshape(groups, block + 2, cols).astype(jnp.float32)
    counts = received[:, block] + received[:, block + 1]
    total = jnp.sum(counts, axis=0)
    average = jnp.sum(counts[:, None, :] * received[:, :block], axis=0) / total
    new_momentum = outer_beta * outer_momentum + average
    new_anchor = anchor - outer_rate * (average + outer_beta * new_momentum)
    return (new_anchor, new_momentum)


def solution(mesh):
    in_specs = (
        P(("island", "fsdp"), None),
        P(("island", "fsdp"), None),
        P(("island", "fsdp"), None),
        P(("island", "fsdp"), None),
        P(("island", "fsdp"), None),
        P("island", "fsdp", None),
        P("island", "fsdp", None),
        P("fsdp", "island"),
        P("fsdp", "island"),
        P("island"),
    )
    out_specs = (P("fsdp", "island"), P("fsdp", "island"))
    return jax.shard_map(
        on_device, mesh=mesh, in_specs=in_specs, out_specs=out_specs, check_vma=False
    )
```

```python
import math

import jax
import jax.numpy as jnp
from jax import lax
from jax.sharding import PartitionSpec as P

KVH = 4
QPK = 8
HD = 128


beta_one = 0.9
beta_two = 0.95
inner_rate = 0.05
decay = 0.1
epsilon = 1e-08
outer_rate = 0.7
outer_beta = 0.9


def attention_weights(query_rows, key_rows, segments):
    length = segments.shape[0]
    queries = query_rows.reshape(length, KVH, QPK, HD)
    keyed = key_rows.reshape(length, KVH, HD)
    scores = jnp.einsum("tgjd,sgd->gjts", queries, keyed, preferred_element_type=jnp.float32) * (
        1.0 / math.sqrt(HD)
    )
    place = jnp.arange(length)
    allowed = (place[None, :] <= place[:, None]) & (segments[:, None] == segments[None, :])
    scores = jnp.where(allowed[None, None], scores, -jnp.inf)
    highest = jnp.max(scores, axis=-1, keepdims=True)
    expo = jnp.exp(scores - highest)
    return (expo / jnp.sum(expo, axis=-1, keepdims=True)).astype(jnp.bfloat16)


def _shift(cols, rows, dx, dz):
    return [
        (a * cols + b, ((a + dx) % rows) * cols + (b + dz) % cols)
        for a in range(rows)
        for b in range(cols)
    ]


def ring_offsets(size):
    return [0, -1, 1, -2][:size] if size == 4 else list(range(0, -size, -1))


def ring_gather(piece, rows, cols):
    def along(part, size, dx, dz):
        if size == 1:
            return [part]
        if size == 4:
            up = lax.ppermute(part, "fsdp", _shift(cols, rows, dx, dz))
            down = lax.ppermute(part, "fsdp", _shift(cols, rows, -dx, -dz))
            far = lax.ppermute(up, "fsdp", _shift(cols, rows, dx, dz))
            return [part, up, down, far]
        got = [part]
        for _ in range(size - 1):
            got.append(lax.ppermute(got[-1], "fsdp", _shift(cols, rows, dx, dz)))
        return got

    row = jnp.concatenate(along(piece, cols, 0, 1), axis=0)
    return jnp.concatenate(along(row, rows, 1, 0), axis=0)


def block_sum(partial, rows, cols):
    me = lax.axis_index("fsdp")
    me_x, me_z = me // cols, me % cols
    tokens = partial.shape[0] // (rows * cols)
    mine = partial.reshape(rows, cols, tokens, partial.shape[1])
    got = []
    for dx in [0, 1, -1, 2]:
        part = lax.dynamic_index_in_dim(mine, (me_x + dx) % rows, axis=0, keepdims=False)
        if dx:
            part = lax.ppermute(part, "fsdp", _shift(cols, rows, dx, 0))
        got.append(part.astype(jnp.float32))
    column = got[0] + got[1] + got[2] + got[3]
    total = None
    for dz in [0, 1, -1, 2]:
        part = lax.dynamic_index_in_dim(column, (me_z + dz) % cols, axis=0, keepdims=False)
        if dz:
            part = lax.ppermute(part, "fsdp", _shift(cols, rows, 0, dz))
        total = part if total is None else total + part
    return total


def on_device(
    hidden,
    query_rows,
    key_rows,
    targets,
    segment_ids,
    first_moment,
    second_moment,
    anchor,
    outer_momentum,
    token_counts,
):
    rows = hidden.shape[0]
    width = key_rows.shape[1]
    members = lax.axis_size("fsdp")
    group_rows = rows * members
    scale_in = 1.0 / math.sqrt(hidden.shape[1])
    attention = attention_weights(query_rows, key_rows, segment_ids[0])
    groups = lax.axis_size("island")
    master = lax.all_gather(anchor, "island", axis=1, tiled=True)
    start_point = master
    block = master.shape[0]
    first = first_moment[0]
    second = second_moment[0]
    feature_rows = lax.all_to_all(hidden, "fsdp", split_axis=1, concat_axis=0, tiled=True)
    grid_cols = 4 if members % 4 == 0 else 1
    grid_rows = members // grid_cols
    me = lax.axis_index("fsdp")
    me_x, me_z = me // grid_cols, me % grid_cols
    take_x = (me_x + jnp.array(ring_offsets(grid_rows))) % grid_rows
    take_z = (me_z + jnp.array(ring_offsets(grid_cols))) % grid_cols
    order = (take_x[:, None] * grid_cols + take_z[None, :]).reshape(-1)
    ring_rows = jnp.take(
        feature_rows.reshape(members, rows, block), order, axis=0
    ).reshape(group_rows, block)
    for inner_step in range(2):
        partial = jnp.dot(
            feature_rows, master.astype(jnp.bfloat16), preferred_element_type=jnp.float32
        ).astype(jnp.bfloat16)
        if grid_rows == 4 and grid_cols == 4:
            projected = block_sum(partial, grid_rows, grid_cols)
        else:
            pieces = lax.all_to_all(
                partial.reshape(members, rows, width), "fsdp", split_axis=0, concat_axis=0, tiled=True
            )
            projected = jnp.sum(pieces.astype(jnp.float32), axis=0)
        values = (projected * scale_in).astype(jnp.bfloat16)
        mixed = jnp.einsum(
            "gjts,sgd->tgjd",
            attention,
            values.reshape(rows, KVH, HD),
            preferred_element_type=jnp.float32,
        )
        error = (
            (mixed.reshape(rows, KVH * QPK * HD) - targets.astype(jnp.float32)) / group_rows
        ).astype(jnp.bfloat16)
        back = jnp.einsum(
            "gjts,tgjd->sgd",
            attention,
            error.reshape(rows, KVH, QPK, HD),
            preferred_element_type=jnp.float32,
        )
        value_grad = (back.reshape(rows, width) * scale_in).astype(jnp.bfloat16)
        grad = lax.dot_general(
            ring_rows,
            ring_gather(value_grad, grid_rows, grid_cols),
            (((0,), (0,)), ((), ())),
            preferred_element_type=jnp.float32,
        )
        first = beta_one * first + (1.0 - beta_one) * grad
        second = beta_two * second + (1.0 - beta_two) * grad * grad
        master = master - inner_rate * (first / (jnp.sqrt(second) + epsilon) + decay * master)
    delta = start_point - master
    cols = anchor.shape[1]
    own_count = token_counts[0].astype(jnp.float32)
    count_high = own_count.astype(jnp.bfloat16)
    count_low = (own_count - count_high.astype(jnp.float32)).astype(jnp.bfloat16)
    sent = jnp.concatenate(
        [
            delta.astype(jnp.bfloat16),
            jnp.full((1, delta.shape[1]), count_high, jnp.bfloat16),
            jnp.full((1, delta.shape[1]), count_low, jnp.bfloat16),
        ],
        axis=0,
    )
    received = lax.all_to_all(
        sent.reshape(block + 2, groups, cols), "island", split_axis=1, concat_axis=0, tiled=True
    ).reshape(groups, block + 2, cols).astype(jnp.float32)
    counts = received[:, block] + received[:, block + 1]
    total = jnp.sum(counts, axis=0)
    average = jnp.sum(counts[:, None, :] * received[:, :block], axis=0) / total
    new_momentum = outer_beta * outer_momentum + average
    new_anchor = anchor - outer_rate * (average + outer_beta * new_momentum)
    return (new_anchor, new_momentum)


def solution(mesh):
    in_specs = (
        P(("island", "fsdp"), None),
        P(("island", "fsdp"), None),
        P(("island", "fsdp"), None),
        P(("island", "fsdp"), None),
        P(("island", "fsdp"), None),
        P("island", "fsdp", None),
        P("island", "fsdp", None),
        P("fsdp", "island"),
        P("fsdp", "island"),
        P("island"),
    )
    out_specs = (P("fsdp", "island"), P("fsdp", "island"))
    return jax.shard_map(
        on_device, mesh=mesh, in_specs=in_specs, out_specs=out_specs, check_vma=False
    )
```

```python
import math

import jax
import jax.numpy as jnp
from jax import lax
from jax.sharding import PartitionSpec as P

KVH = 4
QPK = 8
HD = 128


beta_one = 0.9
beta_two = 0.95
inner_rate = 0.05
decay = 0.1
epsilon = 1e-08
outer_rate = 0.7
outer_beta = 0.9


def attention_weights(query_rows, key_rows, segments):
    length = segments.shape[0]
    queries = query_rows.reshape(length, KVH, QPK, HD)
    keyed = key_rows.reshape(length, KVH, HD)
    scores = jnp.einsum("tgjd,sgd->gjts", queries, keyed, preferred_element_type=jnp.float32) * (
        1.0 / math.sqrt(HD)
    )
    place = jnp.arange(length)
    allowed = (place[None, :] <= place[:, None]) & (segments[:, None] == segments[None, :])
    scores = jnp.where(allowed[None, None], scores, -jnp.inf)
    highest = jnp.max(scores, axis=-1, keepdims=True)
    expo = jnp.exp(scores - highest)
    return (expo / jnp.sum(expo, axis=-1, keepdims=True)).astype(jnp.bfloat16)


def _shift(cols, rows, dx, dz):
    return [
        (a * cols + b, ((a + dx) % rows) * cols + (b + dz) % cols)
        for a in range(rows)
        for b in range(cols)
    ]


def ring_offsets(size):
    return [0, -1, 1, -2][:size] if size == 4 else list(range(0, -size, -1))


def ring_gather(piece, rows, cols):
    def along(part, size, dx, dz):
        if size == 1:
            return [part]
        if size == 4:
            up = lax.ppermute(part, "fsdp", _shift(cols, rows, dx, dz))
            down = lax.ppermute(part, "fsdp", _shift(cols, rows, -dx, -dz))
            far = lax.ppermute(up, "fsdp", _shift(cols, rows, dx, dz))
            return [part, up, down, far]
        got = [part]
        for _ in range(size - 1):
            got.append(lax.ppermute(got[-1], "fsdp", _shift(cols, rows, dx, dz)))
        return got

    row = jnp.concatenate(along(piece, cols, 0, 1), axis=0)
    return jnp.concatenate(along(row, rows, 1, 0), axis=0)


def island_gather(block, sizes):
    strides = [math.prod(sizes[k + 1 :]) for k in range(len(sizes))]
    total = math.prod(sizes)
    me = lax.axis_index("island")
    coords = [(me // strides[k]) % sizes[k] for k in range(len(sizes))]

    def shift(axis, step):
        pairs = []
        for src in range(total):
            at = (src // strides[axis]) % sizes[axis]
            pairs.append((src, src + (((at + step) % sizes[axis]) - at) * strides[axis]))
        return pairs

    pieces = [block]
    sources = [me]
    for axis in reversed(range(len(sizes))):
        size = sizes[axis]
        steps = [0, -1, 1, -2] if size == 4 else list(range(0, -size, -1))
        moved = {0: jnp.stack(pieces, axis=0)}
        if size == 4:
            moved[-1] = lax.ppermute(moved[0], "island", shift(axis, 1))
            moved[1] = lax.ppermute(moved[0], "island", shift(axis, -1))
            moved[-2] = lax.ppermute(moved[-1], "island", shift(axis, 1))
        else:
            for k in range(1, size):
                moved[-k] = lax.ppermute(moved[-k + 1], "island", shift(axis, 1))
        pieces = [moved[o][n] for o in steps for n in range(len(pieces))]
        sources = [
            src + ((coords[axis] + o) % size - coords[axis]) * strides[axis]
            for o in steps
            for src in sources
        ]
    got = jnp.take(jnp.stack(pieces, axis=0), jnp.argsort(jnp.stack(sources)), axis=0)
    return jnp.moveaxis(got, 0, -2).reshape(block.shape[:-1] + (total * block.shape[-1],))


def on_device(
    hidden,
    query_rows,
    key_rows,
    targets,
    segment_ids,
    first_moment,
    second_moment,
    anchor,
    outer_momentum,
    token_counts,
):
    rows = hidden.shape[0]
    width = key_rows.shape[1]
    members = lax.axis_size("fsdp")
    group_rows = rows * members
    scale_in = 1.0 / math.sqrt(hidden.shape[1])
    attention = attention_weights(query_rows, key_rows, segment_ids[0])
    groups = lax.axis_size("island")
    if groups == 32:
        master = island_gather(anchor, (4, 4, 2))
    else:
        master = lax.all_gather(anchor, "island", axis=1, tiled=True)
    start_point = master
    block = master.shape[0]
    first = first_moment[0]
    second = second_moment[0]
    feature_rows = lax.all_to_all(hidden, "fsdp", split_axis=1, concat_axis=0, tiled=True)
    grid_cols = 4 if members % 4 == 0 else 1
    grid_rows = members // grid_cols
    me = lax.axis_index("fsdp")
    me_x, me_z = me // grid_cols, me % grid_cols
    take_x = (me_x + jnp.array(ring_offsets(grid_rows))) % grid_rows
    take_z = (me_z + jnp.array(ring_offsets(grid_cols))) % grid_cols
    order = (take_x[:, None] * grid_cols + take_z[None, :]).reshape(-1)
    ring_rows = jnp.take(
        feature_rows.reshape(members, rows, block), order, axis=0
    ).reshape(group_rows, block)
    for inner_step in range(2):
        partial = jnp.dot(
            feature_rows, master.astype(jnp.bfloat16), preferred_element_type=jnp.float32
        ).astype(jnp.bfloat16)
        pieces = lax.all_to_all(
            partial.reshape(members, rows, width), "fsdp", split_axis=0, concat_axis=0, tiled=True
        )
        projected = jnp.sum(pieces.astype(jnp.float32), axis=0)
        values = (projected * scale_in).astype(jnp.bfloat16)
        mixed = jnp.einsum(
            "gjts,sgd->tgjd",
            attention,
            values.reshape(rows, KVH, HD),
            preferred_element_type=jnp.float32,
        )
        error = (
            (mixed.reshape(rows, KVH * QPK * HD) - targets.astype(jnp.float32)) / group_rows
        ).astype(jnp.bfloat16)
        back = jnp.einsum(
            "gjts,tgjd->sgd",
            attention,
            error.reshape(rows, KVH, QPK, HD),
            preferred_element_type=jnp.float32,
        )
        value_grad = (back.reshape(rows, width) * scale_in).astype(jnp.bfloat16)
        grad = lax.dot_general(
            ring_rows,
            ring_gather(value_grad, grid_rows, grid_cols),
            (((0,), (0,)), ((), ())),
            preferred_element_type=jnp.float32,
        )
        first = beta_one * first + (1.0 - beta_one) * grad
        second = beta_two * second + (1.0 - beta_two) * grad * grad
        master = master - inner_rate * (first / (jnp.sqrt(second) + epsilon) + decay * master)
    delta = start_point - master
    cols = anchor.shape[1]
    own_count = token_counts[0].astype(jnp.float32)
    count_high = own_count.astype(jnp.bfloat16)
    count_low = (own_count - count_high.astype(jnp.float32)).astype(jnp.bfloat16)
    sent = jnp.concatenate(
        [
            delta.astype(jnp.bfloat16),
            jnp.full((1, delta.shape[1]), count_high, jnp.bfloat16),
            jnp.full((1, delta.shape[1]), count_low, jnp.bfloat16),
        ],
        axis=0,
    )
    received = lax.all_to_all(
        sent.reshape(block + 2, groups, cols), "island", split_axis=1, concat_axis=0, tiled=True
    ).reshape(groups, block + 2, cols).astype(jnp.float32)
    counts = received[:, block] + received[:, block + 1]
    total = jnp.sum(counts, axis=0)
    average = jnp.sum(counts[:, None, :] * received[:, :block], axis=0) / total
    new_momentum = outer_beta * outer_momentum + average
    new_anchor = anchor - outer_rate * (average + outer_beta * new_momentum)
    return (new_anchor, new_momentum)


def solution(mesh):
    in_specs = (
        P(("island", "fsdp"), None),
        P(("island", "fsdp"), None),
        P(("island", "fsdp"), None),
        P(("island", "fsdp"), None),
        P(("island", "fsdp"), None),
        P("island", "fsdp", None),
        P("island", "fsdp", None),
        P("fsdp", "island"),
        P("fsdp", "island"),
        P("island"),
    )
    out_specs = (P("fsdp", "island"), P("fsdp", "island"))
    return jax.shard_map(
        on_device, mesh=mesh, in_specs=in_specs, out_specs=out_specs, check_vma=False
    )
```

```python
import math

import jax
import jax.numpy as jnp
from jax import lax
from jax.sharding import PartitionSpec as P

KVH = 4
QPK = 8
HD = 128


beta_one = 0.9
beta_two = 0.95
inner_rate = 0.05
decay = 0.1
epsilon = 1e-08
outer_rate = 0.7
outer_beta = 0.9


def attention_weights(query_rows, key_rows, segments):
    length = segments.shape[0]
    queries = query_rows.reshape(length, KVH, QPK, HD)
    keyed = key_rows.reshape(length, KVH, HD)
    scores = jnp.einsum("tgjd,sgd->gjts", queries, keyed, preferred_element_type=jnp.float32) * (
        1.0 / math.sqrt(HD)
    )
    place = jnp.arange(length)
    allowed = (place[None, :] <= place[:, None]) & (segments[:, None] == segments[None, :])
    scores = jnp.where(allowed[None, None], scores, -jnp.inf)
    highest = jnp.max(scores, axis=-1, keepdims=True)
    expo = jnp.exp(scores - highest)
    return (expo / jnp.sum(expo, axis=-1, keepdims=True)).astype(jnp.bfloat16)


def _shift(cols, rows, dx, dz):
    return [
        (a * cols + b, ((a + dx) % rows) * cols + (b + dz) % cols)
        for a in range(rows)
        for b in range(cols)
    ]


def ring_offsets(size):
    return [0, -1, 1, -2][:size] if size == 4 else list(range(0, -size, -1))


def ring_gather(piece, rows, cols):
    def along(part, size, dx, dz):
        if size == 1:
            return [part]
        if size == 4:
            up = lax.ppermute(part, "fsdp", _shift(cols, rows, dx, dz))
            down = lax.ppermute(part, "fsdp", _shift(cols, rows, -dx, -dz))
            far = lax.ppermute(up, "fsdp", _shift(cols, rows, dx, dz))
            return [part, up, down, far]
        got = [part]
        for _ in range(size - 1):
            got.append(lax.ppermute(got[-1], "fsdp", _shift(cols, rows, dx, dz)))
        return got

    row = jnp.concatenate(along(piece, cols, 0, 1), axis=0)
    return jnp.concatenate(along(row, rows, 1, 0), axis=0)


def island_gather(block, sizes):
    strides = [math.prod(sizes[k + 1 :]) for k in range(len(sizes))]
    total = math.prod(sizes)
    me = lax.axis_index("island")
    coords = [(me // strides[k]) % sizes[k] for k in range(len(sizes))]

    def shift(axis, step):
        pairs = []
        for src in range(total):
            at = (src // strides[axis]) % sizes[axis]
            pairs.append((src, src + (((at + step) % sizes[axis]) - at) * strides[axis]))
        return pairs

    pieces = [block]
    sources = [me]
    for axis in reversed(range(len(sizes))):
        size = sizes[axis]
        steps = [0, -1, 1, -2] if size == 4 else list(range(0, -size, -1))
        moved = {0: jnp.stack(pieces, axis=0)}
        if size == 4:
            moved[-1] = lax.ppermute(moved[0], "island", shift(axis, 1))
            moved[1] = lax.ppermute(moved[0], "island", shift(axis, -1))
            moved[-2] = lax.ppermute(moved[-1], "island", shift(axis, 1))
        else:
            for k in range(1, size):
                moved[-k] = lax.ppermute(moved[-k + 1], "island", shift(axis, 1))
        pieces = [moved[o][n] for o in steps for n in range(len(pieces))]
        sources = [
            src + ((coords[axis] + o) % size - coords[axis]) * strides[axis]
            for o in steps
            for src in sources
        ]
    got = jnp.take(jnp.stack(pieces, axis=0), jnp.argsort(jnp.stack(sources)), axis=0)
    return jnp.moveaxis(got, 0, -2).reshape(block.shape[:-1] + (total * block.shape[-1],))


def on_device(
    hidden,
    query_rows,
    key_rows,
    targets,
    segment_ids,
    first_moment,
    second_moment,
    anchor,
    outer_momentum,
    token_counts,
):
    rows = hidden.shape[0]
    width = key_rows.shape[1]
    members = lax.axis_size("fsdp")
    group_rows = rows * members
    scale_in = 1.0 / math.sqrt(hidden.shape[1])
    attention = attention_weights(query_rows, key_rows, segment_ids[0])
    groups = lax.axis_size("island")
    if groups == 32:
        master = island_gather(anchor, (4, 4, 2))
    else:
        master = lax.all_gather(anchor, "island", axis=1, tiled=True)
    start_point = master
    block = master.shape[0]
    first = first_moment[0]
    second = second_moment[0]
    feature_rows = lax.all_to_all(hidden, "fsdp", split_axis=1, concat_axis=0, tiled=True)
    grid_cols = 4 if members % 4 == 0 else 1
    grid_rows = members // grid_cols
    me = lax.axis_index("fsdp")
    me_x, me_z = me // grid_cols, me % grid_cols
    take_x = (me_x + jnp.array(ring_offsets(grid_rows))) % grid_rows
    take_z = (me_z + jnp.array(ring_offsets(grid_cols))) % grid_cols
    order = (take_x[:, None] * grid_cols + take_z[None, :]).reshape(-1)
    ring_rows = jnp.take(
        feature_rows.reshape(members, rows, block), order, axis=0
    ).reshape(group_rows, block)
    feature_rows, attention = lax.optimization_barrier((feature_rows, attention))
    for inner_step in range(2):
        partial = jnp.dot(
            feature_rows, master.astype(jnp.bfloat16), preferred_element_type=jnp.float32
        ).astype(jnp.bfloat16)
        pieces = lax.all_to_all(
            partial.reshape(members, rows, width), "fsdp", split_axis=0, concat_axis=0, tiled=True
        )
        projected = jnp.sum(pieces.astype(jnp.float32), axis=0)
        values = (projected * scale_in).astype(jnp.bfloat16)
        mixed = jnp.einsum(
            "gjts,sgd->tgjd",
            attention,
            values.reshape(rows, KVH, HD),
            preferred_element_type=jnp.float32,
        )
        error = (
            (mixed.reshape(rows, KVH * QPK * HD) - targets.astype(jnp.float32)) / group_rows
        ).astype(jnp.bfloat16)
        back = jnp.einsum(
            "gjts,tgjd->sgd",
            attention,
            error.reshape(rows, KVH, QPK, HD),
            preferred_element_type=jnp.float32,
        )
        value_grad = (back.reshape(rows, width) * scale_in).astype(jnp.bfloat16)
        grad = lax.dot_general(
            ring_rows,
            ring_gather(value_grad, grid_rows, grid_cols),
            (((0,), (0,)), ((), ())),
            preferred_element_type=jnp.float32,
        )
        first = beta_one * first + (1.0 - beta_one) * grad
        second = beta_two * second + (1.0 - beta_two) * grad * grad
        master = master - inner_rate * (first / (jnp.sqrt(second) + epsilon) + decay * master)
    delta = start_point - master
    cols = anchor.shape[1]
    own_count = token_counts[0].astype(jnp.float32)
    count_high = own_count.astype(jnp.bfloat16)
    count_low = (own_count - count_high.astype(jnp.float32)).astype(jnp.bfloat16)
    sent = jnp.concatenate(
        [
            delta.astype(jnp.bfloat16),
            jnp.full((1, delta.shape[1]), count_high, jnp.bfloat16),
            jnp.full((1, delta.shape[1]), count_low, jnp.bfloat16),
        ],
        axis=0,
    )
    received = lax.all_to_all(
        sent.reshape(block + 2, groups, cols), "island", split_axis=1, concat_axis=0, tiled=True
    ).reshape(groups, block + 2, cols).astype(jnp.float32)
    counts = received[:, block] + received[:, block + 1]
    total = jnp.sum(counts, axis=0)
    average = jnp.sum(counts[:, None, :] * received[:, :block], axis=0) / total
    new_momentum = outer_beta * outer_momentum + average
    new_anchor = anchor - outer_rate * (average + outer_beta * new_momentum)
    return (new_anchor, new_momentum)


def solution(mesh):
    in_specs = (
        P(("island", "fsdp"), None),
        P(("island", "fsdp"), None),
        P(("island", "fsdp"), None),
        P(("island", "fsdp"), None),
        P(("island", "fsdp"), None),
        P("island", "fsdp", None),
        P("island", "fsdp", None),
        P("fsdp", "island"),
        P("fsdp", "island"),
        P("island"),
    )
    out_specs = (P("fsdp", "island"), P("fsdp", "island"))
    return jax.shard_map(
        on_device, mesh=mesh, in_specs=in_specs, out_specs=out_specs, check_vma=False
    )
```

```python
import math

import jax
import jax.numpy as jnp
from jax import lax
from jax.sharding import PartitionSpec as P

KVH = 4
QPK = 8
HD = 128


beta_one = 0.9
beta_two = 0.95
inner_rate = 0.05
decay = 0.1
epsilon = 1e-08
outer_rate = 0.7
outer_beta = 0.9


def attention_weights(query_rows, key_rows, segments):
    length = segments.shape[0]
    queries = query_rows.reshape(length, KVH, QPK, HD)
    keyed = key_rows.reshape(length, KVH, HD)
    scores = jnp.einsum("tgjd,sgd->gjts", queries, keyed, preferred_element_type=jnp.float32) * (
        1.0 / math.sqrt(HD)
    )
    place = jnp.arange(length)
    allowed = (place[None, :] <= place[:, None]) & (segments[:, None] == segments[None, :])
    scores = jnp.where(allowed[None, None], scores, -jnp.inf)
    highest = jnp.max(scores, axis=-1, keepdims=True)
    expo = jnp.exp(scores - highest)
    return (expo / jnp.sum(expo, axis=-1, keepdims=True)).astype(jnp.bfloat16)


def _shift(cols, rows, dx, dz):
    return [
        (a * cols + b, ((a + dx) % rows) * cols + (b + dz) % cols)
        for a in range(rows)
        for b in range(cols)
    ]


def ring_offsets(size):
    return [0, -1, 1, -2][:size] if size == 4 else list(range(0, -size, -1))


def ring_gather(piece, rows, cols):
    def along(part, size, dx, dz):
        if size == 1:
            return [part]
        if size == 4:
            up = lax.ppermute(part, "fsdp", _shift(cols, rows, dx, dz))
            down = lax.ppermute(part, "fsdp", _shift(cols, rows, -dx, -dz))
            far = lax.ppermute(up, "fsdp", _shift(cols, rows, dx, dz))
            return [part, up, down, far]
        got = [part]
        for _ in range(size - 1):
            got.append(lax.ppermute(got[-1], "fsdp", _shift(cols, rows, dx, dz)))
        return got

    row = jnp.concatenate(along(piece, cols, 0, 1), axis=0)
    return jnp.concatenate(along(row, rows, 1, 0), axis=0)


def island_gather(block, sizes):
    strides = [math.prod(sizes[k + 1 :]) for k in range(len(sizes))]
    total = math.prod(sizes)
    me = lax.axis_index("island")
    coords = [(me // strides[k]) % sizes[k] for k in range(len(sizes))]

    def shift(axis, step):
        pairs = []
        for src in range(total):
            at = (src // strides[axis]) % sizes[axis]
            pairs.append((src, src + (((at + step) % sizes[axis]) - at) * strides[axis]))
        return pairs

    pieces = [block]
    sources = [me]
    for axis in reversed(range(len(sizes))):
        size = sizes[axis]
        steps = [0, -1, 1, -2] if size == 4 else list(range(0, -size, -1))
        moved = {0: jnp.stack(pieces, axis=0)}
        if size == 4:
            moved[-1] = lax.ppermute(moved[0], "island", shift(axis, 1))
            moved[1] = lax.ppermute(moved[0], "island", shift(axis, -1))
            moved[-2] = lax.ppermute(moved[0], "island", shift(axis, 2))
        else:
            for k in range(1, size):
                moved[-k] = lax.ppermute(moved[-k + 1], "island", shift(axis, 1))
        pieces = [moved[o][n] for o in steps for n in range(len(pieces))]
        sources = [
            src + ((coords[axis] + o) % size - coords[axis]) * strides[axis]
            for o in steps
            for src in sources
        ]
    got = jnp.take(jnp.stack(pieces, axis=0), jnp.argsort(jnp.stack(sources)), axis=0)
    return jnp.moveaxis(got, 0, -2).reshape(block.shape[:-1] + (total * block.shape[-1],))


def on_device(
    hidden,
    query_rows,
    key_rows,
    targets,
    segment_ids,
    first_moment,
    second_moment,
    anchor,
    outer_momentum,
    token_counts,
):
    rows = hidden.shape[0]
    width = key_rows.shape[1]
    members = lax.axis_size("fsdp")
    group_rows = rows * members
    scale_in = 1.0 / math.sqrt(hidden.shape[1])
    attention = attention_weights(query_rows, key_rows, segment_ids[0])
    groups = lax.axis_size("island")
    if groups == 32:
        master = island_gather(anchor, (4, 4, 2))
    else:
        master = lax.all_gather(anchor, "island", axis=1, tiled=True)
    start_point = master
    block = master.shape[0]
    first = first_moment[0]
    second = second_moment[0]
    feature_rows = lax.all_to_all(hidden, "fsdp", split_axis=1, concat_axis=0, tiled=True)
    grid_cols = 4 if members % 4 == 0 else 1
    grid_rows = members // grid_cols
    me = lax.axis_index("fsdp")
    me_x, me_z = me // grid_cols, me % grid_cols
    take_x = (me_x + jnp.array(ring_offsets(grid_rows))) % grid_rows
    take_z = (me_z + jnp.array(ring_offsets(grid_cols))) % grid_cols
    order = (take_x[:, None] * grid_cols + take_z[None, :]).reshape(-1)
    ring_rows = jnp.take(
        feature_rows.reshape(members, rows, block), order, axis=0
    ).reshape(group_rows, block)
    feature_rows, attention = lax.optimization_barrier((feature_rows, attention))
    for inner_step in range(2):
        partial = jnp.dot(
            feature_rows, master.astype(jnp.bfloat16), preferred_element_type=jnp.float32
        ).astype(jnp.bfloat16)
        pieces = lax.all_to_all(
            partial.reshape(members, rows, width), "fsdp", split_axis=0, concat_axis=0, tiled=True
        )
        projected = jnp.sum(pieces.astype(jnp.float32), axis=0)
        values = (projected * scale_in).astype(jnp.bfloat16)
        mixed = jnp.einsum(
            "gjts,sgd->tgjd",
            attention,
            values.reshape(rows, KVH, HD),
            preferred_element_type=jnp.float32,
        )
        error = (
            (mixed.reshape(rows, KVH * QPK * HD) - targets.astype(jnp.float32)) / group_rows
        ).astype(jnp.bfloat16)
        back = jnp.einsum(
            "gjts,tgjd->sgd",
            attention,
            error.reshape(rows, KVH, QPK, HD),
            preferred_element_type=jnp.float32,
        )
        value_grad = (back.reshape(rows, width) * scale_in).astype(jnp.bfloat16)
        grad = lax.dot_general(
            ring_rows,
            ring_gather(value_grad, grid_rows, grid_cols),
            (((0,), (0,)), ((), ())),
            preferred_element_type=jnp.float32,
        )
        first = beta_one * first + (1.0 - beta_one) * grad
        second = beta_two * second + (1.0 - beta_two) * grad * grad
        master = master - inner_rate * (first / (jnp.sqrt(second) + epsilon) + decay * master)
    delta = start_point - master
    cols = anchor.shape[1]
    own_count = token_counts[0].astype(jnp.float32)
    count_high = own_count.astype(jnp.bfloat16)
    count_low = (own_count - count_high.astype(jnp.float32)).astype(jnp.bfloat16)
    sent = jnp.concatenate(
        [
            delta.astype(jnp.bfloat16),
            jnp.full((1, delta.shape[1]), count_high, jnp.bfloat16),
            jnp.full((1, delta.shape[1]), count_low, jnp.bfloat16),
        ],
        axis=0,
    )
    received = lax.all_to_all(
        sent.reshape(block + 2, groups, cols), "island", split_axis=1, concat_axis=0, tiled=True
    ).reshape(groups, block + 2, cols).astype(jnp.float32)
    counts = received[:, block] + received[:, block + 1]
    total = jnp.sum(counts, axis=0)
    average = jnp.sum(counts[:, None, :] * received[:, :block], axis=0) / total
    new_momentum = outer_beta * outer_momentum + average
    new_anchor = anchor - outer_rate * (average + outer_beta * new_momentum)
    return (new_anchor, new_momentum)


def solution(mesh):
    in_specs = (
        P(("island", "fsdp"), None),
        P(("island", "fsdp"), None),
        P(("island", "fsdp"), None),
        P(("island", "fsdp"), None),
        P(("island", "fsdp"), None),
        P("island", "fsdp", None),
        P("island", "fsdp", None),
        P("fsdp", "island"),
        P("fsdp", "island"),
        P("island"),
    )
    out_specs = (P("fsdp", "island"), P("fsdp", "island"))
    return jax.shard_map(
        on_device, mesh=mesh, in_specs=in_specs, out_specs=out_specs, check_vma=False
    )
```

```python
import math

import jax
import jax.numpy as jnp
from jax import lax
from jax.sharding import PartitionSpec as P

KVH = 4
QPK = 8
HD = 128


beta_one = 0.9
beta_two = 0.95
inner_rate = 0.05
decay = 0.1
epsilon = 1e-08
outer_rate = 0.7
outer_beta = 0.9


def attention_weights(query_rows, key_rows, segments):
    length = segments.shape[0]
    queries = query_rows.reshape(length, KVH, QPK, HD)
    keyed = key_rows.reshape(length, KVH, HD)
    scores = jnp.einsum("tgjd,sgd->gjts", queries, keyed, preferred_element_type=jnp.float32) * (
        1.0 / math.sqrt(HD)
    )
    place = jnp.arange(length)
    allowed = (place[None, :] <= place[:, None]) & (segments[:, None] == segments[None, :])
    scores = jnp.where(allowed[None, None], scores, -jnp.inf)
    highest = jnp.max(scores, axis=-1, keepdims=True)
    expo = jnp.exp(scores - highest)
    return (expo / jnp.sum(expo, axis=-1, keepdims=True)).astype(jnp.bfloat16)


def _shift(cols, rows, dx, dz):
    return [
        (a * cols + b, ((a + dx) % rows) * cols + (b + dz) % cols)
        for a in range(rows)
        for b in range(cols)
    ]


def ring_offsets(size):
    return [0, -1, 1, -2][:size] if size == 4 else list(range(0, -size, -1))


def ring_gather(piece, rows, cols):
    def along(part, size, dx, dz):
        if size == 1:
            return [part]
        if size == 4:
            up = lax.ppermute(part, "fsdp", _shift(cols, rows, dx, dz))
            down = lax.ppermute(part, "fsdp", _shift(cols, rows, -dx, -dz))
            far = lax.ppermute(part, "fsdp", _shift(cols, rows, 2 * dx, 2 * dz))
            return [part, up, down, far]
        got = [part]
        for _ in range(size - 1):
            got.append(lax.ppermute(got[-1], "fsdp", _shift(cols, rows, dx, dz)))
        return got

    row = jnp.concatenate(along(piece, cols, 0, 1), axis=0)
    return jnp.concatenate(along(row, rows, 1, 0), axis=0)


def island_gather(block, sizes):
    strides = [math.prod(sizes[k + 1 :]) for k in range(len(sizes))]
    total = math.prod(sizes)
    me = lax.axis_index("island")
    coords = [(me // strides[k]) % sizes[k] for k in range(len(sizes))]

    def shift(axis, step):
        pairs = []
        for src in range(total):
            at = (src // strides[axis]) % sizes[axis]
            pairs.append((src, src + (((at + step) % sizes[axis]) - at) * strides[axis]))
        return pairs

    pieces = [block]
    sources = [me]
    for axis in reversed(range(len(sizes))):
        size = sizes[axis]
        steps = [0, -1, 1, -2] if size == 4 else list(range(0, -size, -1))
        moved = {0: jnp.stack(pieces, axis=0)}
        if size == 4:
            moved[-1] = lax.ppermute(moved[0], "island", shift(axis, 1))
            moved[1] = lax.ppermute(moved[0], "island", shift(axis, -1))
            moved[-2] = lax.ppermute(moved[0], "island", shift(axis, 2))
        else:
            for k in range(1, size):
                moved[-k] = lax.ppermute(moved[-k + 1], "island", shift(axis, 1))
        pieces = [moved[o][n] for o in steps for n in range(len(pieces))]
        sources = [
            src + ((coords[axis] + o) % size - coords[axis]) * strides[axis]
            for o in steps
            for src in sources
        ]
    got = jnp.take(jnp.stack(pieces, axis=0), jnp.argsort(jnp.stack(sources)), axis=0)
    return jnp.moveaxis(got, 0, -2).reshape(block.shape[:-1] + (total * block.shape[-1],))


def on_device(
    hidden,
    query_rows,
    key_rows,
    targets,
    segment_ids,
    first_moment,
    second_moment,
    anchor,
    outer_momentum,
    token_counts,
):
    rows = hidden.shape[0]
    width = key_rows.shape[1]
    members = lax.axis_size("fsdp")
    group_rows = rows * members
    scale_in = 1.0 / math.sqrt(hidden.shape[1])
    attention = attention_weights(query_rows, key_rows, segment_ids[0])
    groups = lax.axis_size("island")
    if groups == 32:
        master = island_gather(anchor, (4, 4, 2))
    else:
        master = lax.all_gather(anchor, "island", axis=1, tiled=True)
    start_point = master
    block = master.shape[0]
    first = first_moment[0]
    second = second_moment[0]
    feature_rows = lax.all_to_all(hidden, "fsdp", split_axis=1, concat_axis=0, tiled=True)
    grid_cols = 4 if members % 4 == 0 else 1
    grid_rows = members // grid_cols
    me = lax.axis_index("fsdp")
    me_x, me_z = me // grid_cols, me % grid_cols
    take_x = (me_x + jnp.array(ring_offsets(grid_rows))) % grid_rows
    take_z = (me_z + jnp.array(ring_offsets(grid_cols))) % grid_cols
    order = (take_x[:, None] * grid_cols + take_z[None, :]).reshape(-1)
    ring_rows = jnp.take(
        feature_rows.reshape(members, rows, block), order, axis=0
    ).reshape(group_rows, block)
    feature_rows, attention = lax.optimization_barrier((feature_rows, attention))
    for inner_step in range(2):
        partial = jnp.dot(
            feature_rows, master.astype(jnp.bfloat16), preferred_element_type=jnp.float32
        ).astype(jnp.bfloat16)
        pieces = lax.all_to_all(
            partial.reshape(members, rows, width), "fsdp", split_axis=0, concat_axis=0, tiled=True
        )
        projected = jnp.sum(pieces.astype(jnp.float32), axis=0)
        values = (projected * scale_in).astype(jnp.bfloat16)
        mixed = jnp.einsum(
            "gjts,sgd->tgjd",
            attention,
            values.reshape(rows, KVH, HD),
            preferred_element_type=jnp.float32,
        )
        error = (
            (mixed.reshape(rows, KVH * QPK * HD) - targets.astype(jnp.float32)) / group_rows
        ).astype(jnp.bfloat16)
        back = jnp.einsum(
            "gjts,tgjd->sgd",
            attention,
            error.reshape(rows, KVH, QPK, HD),
            preferred_element_type=jnp.float32,
        )
        value_grad = (back.reshape(rows, width) * scale_in).astype(jnp.bfloat16)
        grad = lax.dot_general(
            ring_rows,
            ring_gather(value_grad, grid_rows, grid_cols),
            (((0,), (0,)), ((), ())),
            preferred_element_type=jnp.float32,
        )
        first = beta_one * first + (1.0 - beta_one) * grad
        second = beta_two * second + (1.0 - beta_two) * grad * grad
        master = master - inner_rate * (first / (jnp.sqrt(second) + epsilon) + decay * master)
    delta = start_point - master
    cols = anchor.shape[1]
    own_count = token_counts[0].astype(jnp.float32)
    count_high = own_count.astype(jnp.bfloat16)
    count_low = (own_count - count_high.astype(jnp.float32)).astype(jnp.bfloat16)
    sent = jnp.concatenate(
        [
            delta.astype(jnp.bfloat16),
            jnp.full((1, delta.shape[1]), count_high, jnp.bfloat16),
            jnp.full((1, delta.shape[1]), count_low, jnp.bfloat16),
        ],
        axis=0,
    )
    received = lax.all_to_all(
        sent.reshape(block + 2, groups, cols), "island", split_axis=1, concat_axis=0, tiled=True
    ).reshape(groups, block + 2, cols).astype(jnp.float32)
    counts = received[:, block] + received[:, block + 1]
    total = jnp.sum(counts, axis=0)
    average = jnp.sum(counts[:, None, :] * received[:, :block], axis=0) / total
    new_momentum = outer_beta * outer_momentum + average
    new_anchor = anchor - outer_rate * (average + outer_beta * new_momentum)
    return (new_anchor, new_momentum)


def solution(mesh):
    in_specs = (
        P(("island", "fsdp"), None),
        P(("island", "fsdp"), None),
        P(("island", "fsdp"), None),
        P(("island", "fsdp"), None),
        P(("island", "fsdp"), None),
        P("island", "fsdp", None),
        P("island", "fsdp", None),
        P("fsdp", "island"),
        P("fsdp", "island"),
        P("island"),
    )
    out_specs = (P("fsdp", "island"), P("fsdp", "island"))
    return jax.shard_map(
        on_device, mesh=mesh, in_specs=in_specs, out_specs=out_specs, check_vma=False
    )
```

```python
import math

import jax
import jax.numpy as jnp
from jax import lax
from jax.sharding import PartitionSpec as P

KVH = 4
QPK = 8
HD = 128


beta_one = 0.9
beta_two = 0.95
inner_rate = 0.05
decay = 0.1
epsilon = 1e-08
outer_rate = 0.7
outer_beta = 0.9


def attention_weights(query_rows, key_rows, segments):
    length = segments.shape[0]
    queries = query_rows.reshape(length, KVH, QPK, HD)
    keyed = key_rows.reshape(length, KVH, HD)
    scores = jnp.einsum("tgjd,sgd->gjts", queries, keyed, preferred_element_type=jnp.float32) * (
        1.0 / math.sqrt(HD)
    )
    place = jnp.arange(length)
    allowed = (place[None, :] <= place[:, None]) & (segments[:, None] == segments[None, :])
    scores = jnp.where(allowed[None, None], scores, -jnp.inf)
    highest = jnp.max(scores, axis=-1, keepdims=True)
    expo = jnp.exp(scores - highest)
    return (expo / jnp.sum(expo, axis=-1, keepdims=True)).astype(jnp.bfloat16)


def _shift(cols, rows, dx, dz):
    return [
        (a * cols + b, ((a + dx) % rows) * cols + (b + dz) % cols)
        for a in range(rows)
        for b in range(cols)
    ]


def ring_offsets(size):
    return [0, -1, 1, -2][:size] if size == 4 else list(range(0, -size, -1))


def ring_gather(piece, rows, cols):
    def along(part, size, dx, dz):
        if size == 1:
            return [part]
        if size == 4:
            up = lax.ppermute(part, "fsdp", _shift(cols, rows, dx, dz))
            down = lax.ppermute(part, "fsdp", _shift(cols, rows, -dx, -dz))
            far = lax.ppermute(up, "fsdp", _shift(cols, rows, dx, dz))
            return [part, up, down, far]
        got = [part]
        for _ in range(size - 1):
            got.append(lax.ppermute(got[-1], "fsdp", _shift(cols, rows, dx, dz)))
        return got

    row = jnp.concatenate(along(piece, cols, 0, 1), axis=0)
    return jnp.concatenate(along(row, rows, 1, 0), axis=0)


def island_gather(block, sizes):
    strides = [math.prod(sizes[k + 1 :]) for k in range(len(sizes))]
    total = math.prod(sizes)
    me = lax.axis_index("island")
    coords = [(me // strides[k]) % sizes[k] for k in range(len(sizes))]

    def shift(axis, step):
        pairs = []
        for src in range(total):
            at = (src // strides[axis]) % sizes[axis]
            pairs.append((src, src + (((at + step) % sizes[axis]) - at) * strides[axis]))
        return pairs

    pieces = [block]
    sources = [me]
    for axis in reversed(range(len(sizes))):
        size = sizes[axis]
        steps = [0, -1, 1, -2] if size == 4 else list(range(0, -size, -1))
        moved = {0: jnp.stack(pieces, axis=0)}
        if size == 4:
            moved[-1] = lax.ppermute(moved[0], "island", shift(axis, 1))
            moved[1] = lax.ppermute(moved[0], "island", shift(axis, -1))
            moved[-2] = lax.ppermute(moved[0], "island", shift(axis, 2))
        else:
            for k in range(1, size):
                moved[-k] = lax.ppermute(moved[-k + 1], "island", shift(axis, 1))
        pieces = [moved[o][n] for o in steps for n in range(len(pieces))]
        sources = [
            src + ((coords[axis] + o) % size - coords[axis]) * strides[axis]
            for o in steps
            for src in sources
        ]
    got = jnp.take(jnp.stack(pieces, axis=0), jnp.argsort(jnp.stack(sources)), axis=0)
    return jnp.moveaxis(got, 0, -2).reshape(block.shape[:-1] + (total * block.shape[-1],))


def on_device(
    hidden,
    query_rows,
    key_rows,
    targets,
    segment_ids,
    first_moment,
    second_moment,
    anchor,
    outer_momentum,
    token_counts,
):
    rows = hidden.shape[0]
    width = key_rows.shape[1]
    members = lax.axis_size("fsdp")
    group_rows = rows * members
    scale_in = 1.0 / math.sqrt(hidden.shape[1])
    attention = attention_weights(query_rows, key_rows, segment_ids[0])
    groups = lax.axis_size("island")
    own_count = token_counts[0].astype(jnp.float32)
    counted = jnp.concatenate(
        [anchor, jnp.full((1, anchor.shape[1]), own_count, jnp.float32)], axis=0
    )
    if groups == 32:
        gathered = island_gather(counted, (4, 4, 2))
    else:
        gathered = lax.all_gather(counted, "island", axis=1, tiled=True)
    master = gathered[: anchor.shape[0]]
    counts = gathered[anchor.shape[0]].reshape(groups, anchor.shape[1])
    start_point = master
    block = master.shape[0]
    first = first_moment[0]
    second = second_moment[0]
    feature_rows = lax.all_to_all(hidden, "fsdp", split_axis=1, concat_axis=0, tiled=True)
    grid_cols = 4 if members % 4 == 0 else 1
    grid_rows = members // grid_cols
    me = lax.axis_index("fsdp")
    me_x, me_z = me // grid_cols, me % grid_cols
    take_x = (me_x + jnp.array(ring_offsets(grid_rows))) % grid_rows
    take_z = (me_z + jnp.array(ring_offsets(grid_cols))) % grid_cols
    order = (take_x[:, None] * grid_cols + take_z[None, :]).reshape(-1)
    ring_rows = jnp.take(
        feature_rows.reshape(members, rows, block), order, axis=0
    ).reshape(group_rows, block)
    feature_rows, attention = lax.optimization_barrier((feature_rows, attention))
    for inner_step in range(2):
        partial = jnp.dot(
            feature_rows, master.astype(jnp.bfloat16), preferred_element_type=jnp.float32
        ).astype(jnp.bfloat16)
        pieces = lax.all_to_all(
            partial.reshape(members, rows, width), "fsdp", split_axis=0, concat_axis=0, tiled=True
        )
        projected = jnp.sum(pieces.astype(jnp.float32), axis=0)
        values = (projected * scale_in).astype(jnp.bfloat16)
        mixed = jnp.einsum(
            "gjts,sgd->tgjd",
            attention,
            values.reshape(rows, KVH, HD),
            preferred_element_type=jnp.float32,
        )
        error = (
            (mixed.reshape(rows, KVH * QPK * HD) - targets.astype(jnp.float32)) / group_rows
        ).astype(jnp.bfloat16)
        back = jnp.einsum(
            "gjts,tgjd->sgd",
            attention,
            error.reshape(rows, KVH, QPK, HD),
            preferred_element_type=jnp.float32,
        )
        value_grad = (back.reshape(rows, width) * scale_in).astype(jnp.bfloat16)
        grad = lax.dot_general(
            ring_rows,
            ring_gather(value_grad, grid_rows, grid_cols),
            (((0,), (0,)), ((), ())),
            preferred_element_type=jnp.float32,
        )
        first = beta_one * first + (1.0 - beta_one) * grad
        second = beta_two * second + (1.0 - beta_two) * grad * grad
        master = master - inner_rate * (first / (jnp.sqrt(second) + epsilon) + decay * master)
    delta = start_point - master
    cols = anchor.shape[1]
    received = lax.all_to_all(
        delta.astype(jnp.bfloat16).reshape(block, groups, cols),
        "island",
        split_axis=1,
        concat_axis=0,
        tiled=True,
    ).reshape(groups, block, cols).astype(jnp.float32)
    total = jnp.sum(counts, axis=0)
    average = jnp.sum(counts[:, None, :] * received, axis=0) / total
    new_momentum = outer_beta * outer_momentum + average
    new_anchor = anchor - outer_rate * (average + outer_beta * new_momentum)
    return (new_anchor, new_momentum)


def solution(mesh):
    in_specs = (
        P(("island", "fsdp"), None),
        P(("island", "fsdp"), None),
        P(("island", "fsdp"), None),
        P(("island", "fsdp"), None),
        P(("island", "fsdp"), None),
        P("island", "fsdp", None),
        P("island", "fsdp", None),
        P("fsdp", "island"),
        P("fsdp", "island"),
        P("island"),
    )
    out_specs = (P("fsdp", "island"), P("fsdp", "island"))
    return jax.shard_map(
        on_device, mesh=mesh, in_specs=in_specs, out_specs=out_specs, check_vma=False
    )
```
